512 devices in a mesh: row: 32 (over z, x), col: 16 (over y, core).
Axes of the slice: x: 4, y: 8, z: 8, core: 2. Of those that a mesh axis runs over, the one named last changes fastest.
Arguments:
- src_points: bfloat16 [512, 64, 1024], P('row', 'col'), may hold values from -1.5 to 1.5
- dst_points: bfloat16 [64, 64, 1024], P('col', 'row'), may hold values from -1.5 to 1.5
- support: int32 [512, 8], P('row'), may hold values from 0 to 63, as said below
- log_src_mass: float32 [512, 1024], P('row'), may hold values from -1 to 1
- log_dst_mass: float32 [64, 1024], P('col'), may hold values from -1 to 1
- dst_potential: float32 [64, 1024], P('col'), may hold values from -4 to 114
Outputs:
- src_potential_new: float32 [512, 1024], P('row')
- dst_potential_new: float32 [64, 1024], P('col')
The draws below stay inside these ranges and needn't reach their ends.
Inputs may be any that keep to these rules, and one draw needn't show every extreme that they name: `support`: each row cluster names 8 different column clusters; column cluster b belongs to col index b // 4; the col indices that one row cluster names lie in 3 cyclically consecutive indices of col, each of them named at least once; every column cluster is named by some row cluster; for every index of row and every index of col, at most 3 of the 16 row clusters of that row index name a column cluster of that col index, and some pair reaches 3.
All inputs are finite; a program needn't handle non-finite values.
Results may differ from the reference program's by a relative error of at most 0.0003.
Values may be sent and summed in bfloat16 or wider, within the bound.
No kernel may reach another device: no remote copies, remote signals or barrier semaphores. Data moves between devices by JAX's collectives and lax.ppermute only.
A program may use at most 64 MiB of HBM per device.

```python
import jax
import jax.numpy as jnp
from jax import lax

DIM = 64
PTS = 1024
K = 8
CCD = 4
RC = 512
CC = 64
N_COL = 16


def draw_support(key, part):
    window = min((K + CCD - 1) // CCD + 1, N_COL)
    places = window * CCD
    keys = jax.random.split(jax.random.fold_in(key, 17), 2)
    clusters = jnp.arange(RC, dtype=jnp.int32)
    first_dev = clusters % N_COL
    forced = clusters // N_COL % CCD
    slots = jnp.arange(places, dtype=jnp.int32)
    slot_dev = slots // CCD
    slot_col = slots % CCD
    picks = jax.random.randint(keys[0], (RC, window), 0, CCD).astype(jnp.int32)
    picks = jnp.where(jnp.arange(window, dtype=jnp.int32)[None, :] == 0, forced[:, None], picks)
    mandatory = (slot_col[None, :] == picks[:, slot_dev]).astype(jnp.int32)
    device = (first_dev[:, None] + slot_dev[None, :]) % N_COL
    hot = (device < max(N_COL // 4, 1)).astype(jnp.int32)
    noise = jax.random.randint(keys[1], (RC, places), 0, 1024).astype(jnp.int32)
    score = (mandatory * 100000 + noise + hot * 600 + (window - slot_dev[None, :]) * 100) * places + slots[None, :]
    unused, idx = lax.top_k(score, K)
    chosen_dev = jnp.take_along_axis(device, idx, axis=1)
    return (chosen_dev * CCD + idx % CCD).astype(jnp.int32)


def draw_dst_potential(key, part):
    keys = jax.random.split(key, 1)
    shape = (CC, PTS)
    return jax.random.truncated_normal(keys[0], -4.0, 4.0, shape, jnp.float32)


def steps_of(stream_key, shape, cuts, smallest, top_value):
    factor_of = 1.0
    for axis_at, shards_of in cuts:
        steps = jax.random.uniform(jax.random.fold_in(jax.random.fold_in(stream_key, 6), axis_at), (shards_of,), jnp.float32, smallest / len(cuts), top_value / len(cuts))
        factor_of = factor_of * jnp.repeat(jnp.exp(steps), shape[axis_at] // shards_of).reshape((-1,) + (1,) * (len(shape) - 1 - axis_at))
    return factor_of


def centred(key, shape, width, most, cuts=(), held_as=jnp.bfloat16):
    drawn = jax.random.normal(key, shape, jnp.float32) * width
    if len(cuts) > 0:
        drawn = steps_of(key, shape, cuts, -0.22, 0.18) * drawn
    return jnp.clip(drawn, min=-most, max=most).astype(held_as)


def setup_inputs(seed: int = 0) -> dict:
    splits = jax.random.split(jax.random.key(seed), 7)
    return {
        "src_points": centred(splits[0], (RC, DIM, PTS), 0.25, 1.5, ((0, 32), (1, 16))),
        "dst_points": centred(splits[1], (CC, DIM, PTS), 0.25, 1.5, ((0, 16), (1, 32))),
        "support": draw_support(jax.random.fold_in(splits[6], 71), 0),
        "log_src_mass": jnp.clip(jax.random.uniform(splits[3], (RC, PTS), jnp.float32, -1.0, 1.0) * steps_of(splits[3], (RC, PTS), ((0, 32),), -0.4, 0.0), -1.0, 1.0),
        "log_dst_mass": jnp.clip(jax.random.uniform(splits[4], (CC, PTS), jnp.float32, -1.0, 1.0) * steps_of(splits[4], (CC, PTS), ((0, 16),), -0.4, 0.0), -1.0, 1.0),
        "dst_potential": draw_dst_potential(jax.random.fold_in(splits[6], 71), 0),
    }


blur_scale = 0.5
floor_value = -1.0e30


def square_norms(points):
    values = points.astype(jnp.float32)
    return jnp.sum(values * values, axis=-2)


def block_costs(src_tile, dst_tiles, src_sq, dst_sq):
    inner_prod = jnp.einsum("dp,kdq->kpq", src_tile.astype(jnp.float32), dst_tiles.astype(jnp.float32))
    return src_sq[None, :, None] + dst_sq[:, None, :] - 2.0 * inner_prod


def reference(src_points, dst_points, support, log_src_mass, log_dst_mass, dst_potential):
    src_sq = square_norms(src_points)
    dst_sq = square_norms(dst_points)

    def row_half(inputs):
        src_tile, tile_sq, chosen, log_mass = inputs
        costs = block_costs(src_tile, dst_points[chosen], tile_sq, dst_sq[chosen])
        scores = (dst_potential[chosen][:, None, :] - costs) / blur_scale
        highest = jnp.max(scores, axis=(0, 2))
        totals = jnp.sum(jnp.exp(scores - highest[None, :, None]), axis=(0, 2))
        return blur_scale * (log_mass - (highest + jnp.log(totals)))

    src_new = lax.map(row_half, (src_points, src_sq, support, log_src_mass))

    def col_half(running, inputs):
        col_high, col_total = running
        src_tile, tile_sq, chosen, row_pot = inputs
        costs = block_costs(src_tile, dst_points[chosen], tile_sq, dst_sq[chosen])
        scores = (row_pot[None, :, None] - costs) / blur_scale
        tile_high = jnp.max(scores, axis=1)
        tile_total = jnp.sum(jnp.exp(scores - tile_high[:, None, :]), axis=1)
        old_high = col_high[chosen]
        old_total = col_total[chosen]
        new_high = jnp.maximum(old_high, tile_high)
        new_total = old_total * jnp.exp(old_high - new_high) + tile_total * jnp.exp(tile_high - new_high)
        return (col_high.at[chosen].set(new_high), col_total.at[chosen].set(new_total)), None

    start_high = jnp.full(dst_potential.shape, floor_value, jnp.float32)
    start_total = jnp.zeros(dst_potential.shape, jnp.float32)
    (col_high, col_total), unused = lax.scan(col_half, (start_high, start_total), (src_points, src_sq, support, src_new))
    dst_new = blur_scale * (log_dst_mass - (col_high + jnp.log(col_total)))
    return (src_new, dst_new)
```

```python
import functools

import jax
import jax.numpy as jnp
from jax import lax
from jax.experimental import pallas as pl
from jax.experimental.pallas import tpu as pltpu
from jax.sharding import PartitionSpec as P

blur_scale = 0.5
floor_value = -1e30
SLOTS = 3
CHUNK = 256


def tile_kernel(lhs_ref, bias_ref, rhs_ref, out_ref):
    reduced = lhs_ref.shape[1]
    kept = rhs_ref.shape[2]
    rhs = rhs_ref[0]

    def chunk(ci, carry):
        high, total = carry
        start = pl.multiple_of(ci * CHUNK, CHUNK)
        left = lhs_ref[0, pl.ds(start, CHUNK), :]
        vals = jnp.dot(left, rhs, preferred_element_type=jnp.float32)
        vals = vals + bias_ref[0, pl.ds(start, CHUNK), :]
        new_high = jnp.maximum(high, jnp.max(vals, axis=0, keepdims=True))
        total = total * jnp.exp(high - new_high) + jnp.sum(
            jnp.exp(vals - new_high), axis=0, keepdims=True
        )
        return new_high, total

    start = (
        jnp.full((1, kept), floor_value, jnp.float32),
        jnp.zeros((1, kept), jnp.float32),
    )
    high, total = lax.fori_loop(0, reduced // CHUNK, chunk, start, unroll=True)
    out_ref[0, 0] = high + jnp.log(total)


def tile_lse(lhs, bias, rhs, lhs_by_slot):
    n_lhs, reduced, depth = lhs.shape
    n_rhs, _, kept = rhs.shape
    slots, n_cc = (n_lhs, n_rhs) if lhs_by_slot else (n_rhs, n_lhs)
    if lhs_by_slot:
        lhs_map = lambda s, k: (s, 0, 0)
        rhs_map = lambda s, k: (k, 0, 0)
    else:
        lhs_map = lambda s, k: (k, 0, 0)
        rhs_map = lambda s, k: (s, 0, 0)
    return pl.pallas_call(
        tile_kernel,
        grid=(slots, n_cc),
        in_specs=[
            pl.BlockSpec((1, reduced, depth), lhs_map),
            pl.BlockSpec((1, reduced, 1), lhs_map),
            pl.BlockSpec((1, depth, kept), rhs_map),
        ],
        out_specs=pl.BlockSpec((1, 1, 1, kept), lambda s, k: (s, k, 0, 0)),
        out_shape=jax.ShapeDtypeStruct((slots, n_cc, 1, kept), jnp.float32),
    )(lhs, bias, rhs)


def masked_lse(values, mask, axis):
    high = jnp.max(jnp.where(mask, values, floor_value), axis=axis)
    total = jnp.sum(
        jnp.where(mask, jnp.exp(values - jnp.expand_dims(high, axis)), 0.0), axis=axis
    )
    return jnp.where(jnp.any(mask, axis=axis), high + jnp.log(total), floor_value)


def log_add(first, second):
    high = jnp.maximum(first, second)
    return high + jnp.log(jnp.exp(first - high) + jnp.exp(second - high))


def body(src_points, dst_points, support, log_src_mass, log_dst_mass, dst_potential, n_row, n_col):
    row_count, dim_part, pts = src_points.shape
    col_count = dst_points.shape[0]
    col_id = lax.axis_index("col")

    dst_full = lax.all_gather(dst_points, "row", axis=1, tiled=True)

    dev_of = support // col_count
    touches = jnp.any(
        dev_of[:, :, None] == jnp.arange(n_col, dtype=jnp.int32)[None, None, :], axis=1
    )
    rank = jnp.cumsum(touches.astype(jnp.int32), axis=0) - 1
    onehot = touches.T[:, None, :] & (
        rank.T[:, None, :] == jnp.arange(SLOTS, dtype=jnp.int32)[None, :, None]
    )
    table = jnp.sum(
        onehot.astype(jnp.int32) * jnp.arange(row_count, dtype=jnp.int32)[None, None, :], axis=2
    )
    slot_ok = jnp.any(onehot, axis=2)

    send = jnp.take(src_points, table.reshape(-1), axis=0).reshape(
        n_col, SLOTS, dim_part, pts
    )
    recv = lax.all_to_all(send, "col", 0, 0, tiled=True)
    src_mine = recv.transpose(1, 0, 2, 3).reshape(SLOTS, n_col * dim_part, pts)

    my_table = lax.dynamic_index_in_dim(table, col_id, 0, keepdims=False)
    my_ok = lax.dynamic_index_in_dim(slot_ok, col_id, 0, keepdims=False)
    my_support = jnp.take(support, my_table, axis=0)
    valid = my_ok[:, None] & jnp.any(
        my_support[:, None, :]
        == (col_id * col_count + jnp.arange(col_count, dtype=jnp.int32))[None, :, None],
        axis=2,
    )

    src_vals = src_mine.astype(jnp.float32)
    src_sq = jnp.sum(src_vals * src_vals, axis=1)
    dst_vals = dst_full.astype(jnp.float32)
    dst_sq = jnp.sum(dst_vals * dst_vals, axis=1)

    dst_lhs = (dst_full * 4).transpose(0, 2, 1)
    dst_bias = (2.0 * dst_potential - 2.0 * dst_sq)[:, :, None]
    row_tiles = tile_lse(dst_lhs, dst_bias, src_mine, lhs_by_slot=False)[:, :, 0, :]
    row_local = masked_lse(row_tiles, valid[:, :, None], axis=1) - 2.0 * src_sq
    row_local = jnp.where(my_ok[:, None], row_local, floor_value)

    row_all = lax.all_gather(row_local, "col", axis=0, tiled=False)
    owner = onehot.transpose(2, 0, 1)
    whole = masked_lse(
        jnp.broadcast_to(row_all[None], (row_count, n_col, SLOTS, pts)).reshape(row_count, n_col * SLOTS, pts),
        owner.reshape(row_count, n_col * SLOTS)[:, :, None],
        axis=1,
    )
    src_new = blur_scale * (log_src_mass - whole)

    my_pot = jnp.take(src_new, my_table, axis=0)
    src_lhs = (src_mine * 4).transpose(0, 2, 1)
    src_bias = (2.0 * my_pot - 2.0 * src_sq)[:, :, None]
    col_tiles = tile_lse(src_lhs, src_bias, dst_full, lhs_by_slot=True)[:, :, 0, :]
    col_local = masked_lse(col_tiles, valid[:, :, None], axis=0)

    step = 1
    while step < n_row:
        partner = lax.ppermute(col_local, "row", [(i, i ^ step) for i in range(n_row)])
        col_local = log_add(col_local, partner)
        step *= 2
    dst_new = blur_scale * (log_dst_mass - (col_local - 2.0 * dst_sq))
    return (src_new, dst_new)


def solution(mesh):
    n_row = mesh.shape["row"]
    n_col = mesh.shape["col"]
    return jax.shard_map(
        functools.partial(body, n_row=n_row, n_col=n_col),
        mesh=mesh,
        in_specs=(
            P("row", "col", None),
            P("col", "row", None),
            P("row", None),
            P("row", None),
            P("col", None),
            P("col", None),
        ),
        out_specs=(P("row", None), P("col", None)),
        check_vma=False,
    )
```

```python
import functools

import jax
import jax.numpy as jnp
from jax import lax
from jax.experimental import pallas as pl
from jax.experimental.pallas import tpu as pltpu
from jax.sharding import PartitionSpec as P

blur_scale = 0.5
floor_value = -1e30
SLOTS = 3
CHUNK = 256


def tile_kernel(lhs_ref, bias_ref, rhs_ref, out_ref):
    reduced = lhs_ref.shape[1]
    kept = rhs_ref.shape[2]
    rhs = rhs_ref[0]

    def chunk(ci, carry):
        high, total = carry
        start = pl.multiple_of(ci * CHUNK, CHUNK)
        left = lhs_ref[0, pl.ds(start, CHUNK), :]
        vals = jnp.dot(left, rhs, preferred_element_type=jnp.float32)
        vals = vals + bias_ref[0, pl.ds(start, CHUNK), :]
        new_high = jnp.maximum(high, jnp.max(vals, axis=0, keepdims=True))
        total = total * jnp.exp(high - new_high) + jnp.sum(
            jnp.exp(vals - new_high), axis=0, keepdims=True
        )
        return new_high, total

    start = (
        jnp.full((1, kept), floor_value, jnp.float32),
        jnp.zeros((1, kept), jnp.float32),
    )
    high, total = lax.fori_loop(0, reduced // CHUNK, chunk, start, unroll=True)
    out_ref[0, 0] = high + jnp.log(total)


def tile_lse(lhs, bias, rhs, lhs_by_slot):
    n_lhs, reduced, depth = lhs.shape
    n_rhs, _, kept = rhs.shape
    slots, n_cc = (n_lhs, n_rhs) if lhs_by_slot else (n_rhs, n_lhs)
    if lhs_by_slot:
        lhs_map = lambda s, k: (s, 0, 0)
        rhs_map = lambda s, k: (k, 0, 0)
    else:
        lhs_map = lambda s, k: (k, 0, 0)
        rhs_map = lambda s, k: (s, 0, 0)
    return pl.pallas_call(
        tile_kernel,
        grid=(slots, n_cc),
        in_specs=[
            pl.BlockSpec((1, reduced, depth), lhs_map),
            pl.BlockSpec((1, reduced, 1), lhs_map),
            pl.BlockSpec((1, depth, kept), rhs_map),
        ],
        out_specs=pl.BlockSpec((1, 1, 1, kept), lambda s, k: (s, k, 0, 0)),
        out_shape=jax.ShapeDtypeStruct((slots, n_cc, 1, kept), jnp.float32),
    )(lhs, bias, rhs)


def masked_lse(values, mask, axis):
    high = jnp.max(jnp.where(mask, values, floor_value), axis=axis)
    total = jnp.sum(
        jnp.where(mask, jnp.exp(values - jnp.expand_dims(high, axis)), 0.0), axis=axis
    )
    return jnp.where(jnp.any(mask, axis=axis), high + jnp.log(total), floor_value)


def log_add(first, second):
    high = jnp.maximum(first, second)
    return high + jnp.log(jnp.exp(first - high) + jnp.exp(second - high))


def body(src_points, dst_points, support, log_src_mass, log_dst_mass, dst_potential, n_row, n_col):
    row_count, dim_part, pts = src_points.shape
    col_count = dst_points.shape[0]
    col_id = lax.axis_index("col")

    dst_copies = jnp.broadcast_to(dst_points[None], (n_row,) + dst_points.shape)
    dst_recv = lax.all_to_all(dst_copies, "row", 0, 0, tiled=True)
    dst_full = dst_recv.transpose(1, 0, 2, 3).reshape(col_count, -1, dst_points.shape[2])

    dev_of = support // col_count
    touches = jnp.any(
        dev_of[:, :, None] == jnp.arange(n_col, dtype=jnp.int32)[None, None, :], axis=1
    )
    rank = jnp.cumsum(touches.astype(jnp.int32), axis=0) - 1
    onehot = touches.T[:, None, :] & (
        rank.T[:, None, :] == jnp.arange(SLOTS, dtype=jnp.int32)[None, :, None]
    )
    table = jnp.sum(
        onehot.astype(jnp.int32) * jnp.arange(row_count, dtype=jnp.int32)[None, None, :], axis=2
    )
    slot_ok = jnp.any(onehot, axis=2)

    send = jnp.take(src_points, table.reshape(-1), axis=0).reshape(
        n_col, SLOTS, dim_part, pts
    )
    recv = lax.all_to_all(send, "col", 0, 0, tiled=True)
    src_mine = recv.transpose(1, 0, 2, 3).reshape(SLOTS, n_col * dim_part, pts)

    my_table = lax.dynamic_index_in_dim(table, col_id, 0, keepdims=False)
    my_ok = lax.dynamic_index_in_dim(slot_ok, col_id, 0, keepdims=False)
    my_support = jnp.take(support, my_table, axis=0)
    valid = my_ok[:, None] & jnp.any(
        my_support[:, None, :]
        == (col_id * col_count + jnp.arange(col_count, dtype=jnp.int32))[None, :, None],
        axis=2,
    )

    src_vals = src_mine.astype(jnp.float32)
    src_sq = jnp.sum(src_vals * src_vals, axis=1)
    dst_vals = dst_full.astype(jnp.float32)
    dst_sq = jnp.sum(dst_vals * dst_vals, axis=1)

    dst_lhs = (dst_full * 4).transpose(0, 2, 1)
    dst_bias = (2.0 * dst_potential - 2.0 * dst_sq)[:, :, None]
    row_tiles = tile_lse(dst_lhs, dst_bias, src_mine, lhs_by_slot=False)[:, :, 0, :]
    row_local = masked_lse(row_tiles, valid[:, :, None], axis=1) - 2.0 * src_sq
    row_local = jnp.where(my_ok[:, None], row_local, floor_value)

    row_all = lax.all_gather(row_local, "col", axis=0, tiled=False)
    owner = onehot.transpose(2, 0, 1)
    whole = masked_lse(
        jnp.broadcast_to(row_all[None], (row_count, n_col, SLOTS, pts)).reshape(row_count, n_col * SLOTS, pts),
        owner.reshape(row_count, n_col * SLOTS)[:, :, None],
        axis=1,
    )
    src_new = blur_scale * (log_src_mass - whole)

    my_pot = jnp.take(src_new, my_table, axis=0)
    src_lhs = (src_mine * 4).transpose(0, 2, 1)
    src_bias = (2.0 * my_pot - 2.0 * src_sq)[:, :, None]
    col_tiles = tile_lse(src_lhs, src_bias, dst_full, lhs_by_slot=True)[:, :, 0, :]
    col_local = masked_lse(col_tiles, valid[:, :, None], axis=0)

    col_copies = jnp.broadcast_to(col_local[None], (n_row,) + col_local.shape)
    col_all = lax.all_to_all(col_copies, "row", 0, 0, tiled=True)
    col_high = jnp.max(col_all, axis=0)
    col_whole = col_high + jnp.log(jnp.sum(jnp.exp(col_all - col_high[None]), axis=0))
    dst_new = blur_scale * (log_dst_mass - (col_whole - 2.0 * dst_sq))
    return (src_new, dst_new)


def solution(mesh):
    n_row = mesh.shape["row"]
    n_col = mesh.shape["col"]
    return jax.shard_map(
        functools.partial(body, n_row=n_row, n_col=n_col),
        mesh=mesh,
        in_specs=(
            P("row", "col", None),
            P("col", "row", None),
            P("row", None),
            P("row", None),
            P("col", None),
            P("col", None),
        ),
        out_specs=(P("row", None), P("col", None)),
        check_vma=False,
    )
```

```python
import functools

import jax
import jax.numpy as jnp
from jax import lax
from jax.experimental import pallas as pl
from jax.experimental.pallas import tpu as pltpu
from jax.sharding import PartitionSpec as P

blur_scale = 0.5
floor_value = -1e30
SLOTS = 3
CHUNK = 256


def tile_kernel(lhs_ref, bias_ref, rhs_ref, out_ref):
    reduced = lhs_ref.shape[2]
    kept = rhs_ref.shape[2]
    rhs = rhs_ref[0]

    def chunk(ci, carry):
        high, total = carry
        start = pl.multiple_of(ci * CHUNK, CHUNK)
        left = lhs_ref[0, :, pl.ds(start, CHUNK)]
        vals = lax.dot_general(
            left, rhs, (((0,), (0,)), ((), ())), preferred_element_type=jnp.float32
        )
        vals = vals + bias_ref[0, pl.ds(start, CHUNK), :]
        new_high = jnp.maximum(high, jnp.max(vals, axis=0, keepdims=True))
        total = total * jnp.exp(high - new_high) + jnp.sum(
            jnp.exp(vals - new_high), axis=0, keepdims=True
        )
        return new_high, total

    start = (
        jnp.full((1, kept), floor_value, jnp.float32),
        jnp.zeros((1, kept), jnp.float32),
    )
    high, total = lax.fori_loop(0, reduced // CHUNK, chunk, start, unroll=True)
    out_ref[0, 0] = high + jnp.log(total)


def tile_lse(lhs, bias, rhs, lhs_by_slot):
    n_lhs, depth, reduced = lhs.shape
    n_rhs, _, kept = rhs.shape
    slots, n_cc = (n_lhs, n_rhs) if lhs_by_slot else (n_rhs, n_lhs)
    if lhs_by_slot:
        lhs_map = lambda s, k: (s, 0, 0)
        rhs_map = lambda s, k: (k, 0, 0)
    else:
        lhs_map = lambda s, k: (k, 0, 0)
        rhs_map = lambda s, k: (s, 0, 0)
    return pl.pallas_call(
        tile_kernel,
        grid=(slots, n_cc),
        in_specs=[
            pl.BlockSpec((1, depth, reduced), lhs_map),
            pl.BlockSpec((1, reduced, 1), lhs_map),
            pl.BlockSpec((1, depth, kept), rhs_map),
        ],
        out_specs=pl.BlockSpec((1, 1, 1, kept), lambda s, k: (s, k, 0, 0)),
        out_shape=jax.ShapeDtypeStruct((slots, n_cc, 1, kept), jnp.float32),
    )(lhs, bias, rhs)


def masked_lse(values, mask, axis):
    high = jnp.max(jnp.where(mask, values, floor_value), axis=axis)
    total = jnp.sum(
        jnp.where(mask, jnp.exp(values - jnp.expand_dims(high, axis)), 0.0), axis=axis
    )
    return jnp.where(jnp.any(mask, axis=axis), high + jnp.log(total), floor_value)


def log_add(first, second):
    high = jnp.maximum(first, second)
    return high + jnp.log(jnp.exp(first - high) + jnp.exp(second - high))


def body(src_points, dst_points, support, log_src_mass, log_dst_mass, dst_potential, n_row, n_col):
    row_count, dim_part, pts = src_points.shape
    col_count = dst_points.shape[0]
    col_id = lax.axis_index("col")

    dst_copies = jnp.broadcast_to(dst_points[None], (n_row,) + dst_points.shape)
    dst_recv = lax.all_to_all(dst_copies, "row", 0, 0, tiled=True)

    dev_of = support // col_count
    touches = jnp.any(
        dev_of[:, :, None] == jnp.arange(n_col, dtype=jnp.int32)[None, None, :], axis=1
    )
    rank = jnp.cumsum(touches.astype(jnp.int32), axis=0) - 1
    onehot = touches.T[:, None, :] & (
        rank.T[:, None, :] == jnp.arange(SLOTS, dtype=jnp.int32)[None, :, None]
    )
    table = jnp.sum(
        onehot.astype(jnp.int32) * jnp.arange(row_count, dtype=jnp.int32)[None, None, :], axis=2
    )
    slot_ok = jnp.any(onehot, axis=2)

    dst_recv, src_points = lax.optimization_barrier((dst_recv, src_points))
    send = jnp.take(src_points, table.reshape(-1), axis=0).reshape(
        n_col, SLOTS, dim_part, pts
    )
    recv = lax.all_to_all(send, "col", 0, 0, tiled=True)
    src_mine = recv.transpose(1, 0, 2, 3).reshape(SLOTS, n_col * dim_part, pts)

    dst_full = dst_recv.transpose(1, 0, 2, 3).reshape(col_count, -1, pts)
    my_table = lax.dynamic_index_in_dim(table, col_id, 0, keepdims=False)
    my_ok = lax.dynamic_index_in_dim(slot_ok, col_id, 0, keepdims=False)
    my_support = jnp.take(support, my_table, axis=0)
    valid = my_ok[:, None] & jnp.any(
        my_support[:, None, :]
        == (col_id * col_count + jnp.arange(col_count, dtype=jnp.int32))[None, :, None],
        axis=2,
    )

    src_vals = src_mine.astype(jnp.float32)
    src_sq = jnp.sum(src_vals * src_vals, axis=1)
    dst_vals = dst_full.astype(jnp.float32)
    dst_sq = jnp.sum(dst_vals * dst_vals, axis=1)

    dst_lhs = dst_full * 4
    dst_bias = (2.0 * dst_potential - 2.0 * dst_sq)[:, :, None]
    row_tiles = tile_lse(dst_lhs, dst_bias, src_mine, lhs_by_slot=False)[:, :, 0, :]
    row_local = masked_lse(row_tiles, valid[:, :, None], axis=1) - 2.0 * src_sq
    row_local = jnp.where(my_ok[:, None], row_local, floor_value)

    row_all = lax.all_gather(row_local, "col", axis=0, tiled=False)
    owner = onehot.transpose(2, 0, 1)
    whole = masked_lse(
        jnp.broadcast_to(row_all[None], (row_count, n_col, SLOTS, pts)).reshape(row_count, n_col * SLOTS, pts),
        owner.reshape(row_count, n_col * SLOTS)[:, :, None],
        axis=1,
    )
    src_new = blur_scale * (log_src_mass - whole)

    my_pot = jnp.take(src_new, my_table, axis=0)
    src_lhs = src_mine * 4
    src_bias = (2.0 * my_pot - 2.0 * src_sq)[:, :, None]
    col_tiles = tile_lse(src_lhs, src_bias, dst_full, lhs_by_slot=True)[:, :, 0, :]
    col_local = masked_lse(col_tiles, valid[:, :, None], axis=0)

    col_copies = jnp.broadcast_to(col_local[None], (n_row,) + col_local.shape)
    col_all = lax.all_to_all(col_copies, "row", 0, 0, tiled=True)
    col_high = jnp.max(col_all, axis=0)
    col_whole = col_high + jnp.log(jnp.sum(jnp.exp(col_all - col_high[None]), axis=0))
    dst_new = blur_scale * (log_dst_mass - (col_whole - 2.0 * dst_sq))
    return (src_new, dst_new)


def solution(mesh):
    n_row = mesh.shape["row"]
    n_col = mesh.shape["col"]
    return jax.shard_map(
        functools.partial(body, n_row=n_row, n_col=n_col),
        mesh=mesh,
        in_specs=(
            P("row", "col", None),
            P("col", "row", None),
            P("row", None),
            P("row", None),
            P("col", None),
            P("col", None),
        ),
        out_specs=(P("row", None), P("col", None)),
        check_vma=False,
    )
```

```python
import functools

import jax
import jax.numpy as jnp
from jax import lax
from jax.experimental import pallas as pl
from jax.experimental.pallas import tpu as pltpu
from jax.sharding import PartitionSpec as P

blur_scale = 0.5
floor_value = -1e30
SLOTS = 3
CHUNK = 256


def tile_kernel(valid_ref, lhs_ref, bias_ref, rhs_ref, sub_ref, out_ref, acc_high, acc_total):
    outer = pl.program_id(0)
    inner = pl.program_id(1)
    n_inner = pl.num_programs(1)
    reduced = lhs_ref.shape[2]
    kept = rhs_ref.shape[2]

    @pl.when(inner == 0)
    def _():
        acc_high[...] = jnp.full((1, kept), floor_value, jnp.float32)
        acc_total[...] = jnp.zeros((1, kept), jnp.float32)

    @pl.when(valid_ref[outer * n_inner + inner] > 0)
    def _():
        rhs = rhs_ref[0]

        def chunk(ci, carry):
            high, total = carry
            start = pl.multiple_of(ci * CHUNK, CHUNK)
            left = lhs_ref[0, :, pl.ds(start, CHUNK)]
            vals = lax.dot_general(
                left, rhs, (((0,), (0,)), ((), ())), preferred_element_type=jnp.float32
            )
            vals = vals + bias_ref[0, pl.ds(start, CHUNK), :]
            new_high = jnp.maximum(high, jnp.max(vals, axis=0, keepdims=True))
            total = total * jnp.exp(high - new_high) + jnp.sum(
                jnp.exp(vals - new_high), axis=0, keepdims=True
            )
            return new_high, total

        start = (
            jnp.full((1, kept), floor_value, jnp.float32),
            jnp.zeros((1, kept), jnp.float32),
        )
        high, total = lax.fori_loop(0, reduced // CHUNK, chunk, start, unroll=True)
        old_high = acc_high[...]
        new_high = jnp.maximum(old_high, high)
        acc_total[...] = acc_total[...] * jnp.exp(old_high - new_high) + total * jnp.exp(
            high - new_high
        )
        acc_high[...] = new_high

    @pl.when(inner == n_inner - 1)
    def _():
        total = acc_total[...]
        found = total > 0.0
        whole = acc_high[...] + jnp.log(jnp.where(found, total, 1.0))
        out_ref[0] = jnp.where(found, whole - sub_ref[0], floor_value)


def tile_lse(valid, lhs, bias, rhs, sub):
    n_in, depth, reduced = lhs.shape
    n_out, _, kept = rhs.shape
    grid_spec = pltpu.PrefetchScalarGridSpec(
        num_scalar_prefetch=1,
        grid=(n_out, n_in),
        in_specs=[
            pl.BlockSpec((1, depth, reduced), lambda o, n, v: (n, 0, 0)),
            pl.BlockSpec((1, reduced, 1), lambda o, n, v: (n, 0, 0)),
            pl.BlockSpec((1, depth, kept), lambda o, n, v: (o, 0, 0)),
            pl.BlockSpec((1, 1, kept), lambda o, n, v: (o, 0, 0)),
        ],
        out_specs=pl.BlockSpec((1, 1, kept), lambda o, n, v: (o, 0, 0)),
        scratch_shapes=[pltpu.VMEM((1, kept), jnp.float32), pltpu.VMEM((1, kept), jnp.float32)],
    )
    return pl.pallas_call(
        tile_kernel,
        grid_spec=grid_spec,
        out_shape=jax.ShapeDtypeStruct((n_out, 1, kept), jnp.float32),
    )(valid, lhs, bias, rhs, sub)


def masked_lse(values, mask, axis):
    high = jnp.max(jnp.where(mask, values, floor_value), axis=axis)
    total = jnp.sum(
        jnp.where(mask, jnp.exp(values - jnp.expand_dims(high, axis)), 0.0), axis=axis
    )
    return jnp.where(jnp.any(mask, axis=axis), high + jnp.log(total), floor_value)


def log_add(first, second):
    high = jnp.maximum(first, second)
    return high + jnp.log(jnp.exp(first - high) + jnp.exp(second - high))


def body(src_points, dst_points, support, log_src_mass, log_dst_mass, dst_potential, n_row, n_col):
    row_count, dim_part, pts = src_points.shape
    col_count = dst_points.shape[0]
    col_id = lax.axis_index("col")

    dst_copies = jnp.broadcast_to(dst_points[None], (n_row,) + dst_points.shape)
    dst_recv = lax.all_to_all(dst_copies, "row", 0, 0, tiled=True)

    dev_of = support // col_count
    touches = jnp.any(
        dev_of[:, :, None] == jnp.arange(n_col, dtype=jnp.int32)[None, None, :], axis=1
    )
    rank = jnp.cumsum(touches.astype(jnp.int32), axis=0) - 1
    onehot = touches.T[:, None, :] & (
        rank.T[:, None, :] == jnp.arange(SLOTS, dtype=jnp.int32)[None, :, None]
    )
    table = jnp.sum(
        onehot.astype(jnp.int32) * jnp.arange(row_count, dtype=jnp.int32)[None, None, :], axis=2
    )
    slot_ok = jnp.any(onehot, axis=2)

    send = jnp.take(src_points, table.reshape(-1), axis=0).reshape(
        n_col, SLOTS, dim_part, pts
    ) * 4
    dst_recv, send = lax.optimization_barrier((dst_recv, send))
    recv = lax.all_to_all(send, "col", 0, 0, tiled=True)
    src_four = recv.transpose(1, 0, 2, 3).reshape(SLOTS, n_col * dim_part, pts)

    dst_full = dst_recv.transpose(1, 0, 2, 3).reshape(col_count, -1, pts)
    my_table = lax.dynamic_index_in_dim(table, col_id, 0, keepdims=False)
    my_ok = lax.dynamic_index_in_dim(slot_ok, col_id, 0, keepdims=False)
    my_support = jnp.take(support, my_table, axis=0)
    valid = my_ok[:, None] & jnp.any(
        my_support[:, None, :]
        == (col_id * col_count + jnp.arange(col_count, dtype=jnp.int32))[None, :, None],
        axis=2,
    )

    src_vals = src_four.astype(jnp.float32)
    src_sq = jnp.sum(src_vals * src_vals, axis=1) / 16.0
    dst_vals = dst_full.astype(jnp.float32)
    dst_sq = jnp.sum(dst_vals * dst_vals, axis=1)

    valid_int = valid.astype(jnp.int32)
    dst_bias = (2.0 * dst_potential - 2.0 * dst_sq)[:, :, None]
    row_local = tile_lse(
        valid_int.reshape(-1), dst_full, dst_bias, src_four, (2.0 * src_sq)[:, None, :]
    )[:, 0, :]
    row_local = jnp.where(my_ok[:, None], row_local, floor_value)

    row_all = lax.all_gather(row_local, "col", axis=0, tiled=False)
    owner = onehot.transpose(2, 0, 1)
    whole = masked_lse(
        jnp.broadcast_to(row_all[None], (row_count, n_col, SLOTS, pts)).reshape(row_count, n_col * SLOTS, pts),
        owner.reshape(row_count, n_col * SLOTS)[:, :, None],
        axis=1,
    )
    src_new = blur_scale * (log_src_mass - whole)

    my_pot = jnp.take(src_new, my_table, axis=0)
    src_bias = (2.0 * my_pot - 2.0 * src_sq)[:, :, None]
    col_local = tile_lse(
        valid_int.T.reshape(-1), src_four, src_bias, dst_full, (2.0 * dst_sq)[:, None, :]
    )[:, 0, :]

    col_copies = jnp.broadcast_to(col_local[None], (n_row,) + col_local.shape)
    col_all = lax.all_to_all(col_copies, "row", 0, 0, tiled=True)
    col_high = jnp.max(col_all, axis=0)
    col_whole = col_high + jnp.log(jnp.sum(jnp.exp(col_all - col_high[None]), axis=0))
    dst_new = blur_scale * (log_dst_mass - col_whole)
    return (src_new, dst_new)


def solution(mesh):
    n_row = mesh.shape["row"]
    n_col = mesh.shape["col"]
    return jax.shard_map(
        functools.partial(body, n_row=n_row, n_col=n_col),
        mesh=mesh,
        in_specs=(
            P("row", "col", None),
            P("col", "row", None),
            P("row", None),
            P("row", None),
            P("col", None),
            P("col", None),
        ),
        out_specs=(P("row", None), P("col", None)),
        check_vma=False,
    )
```

```python
import functools

import jax
import jax.numpy as jnp
from jax import lax
from jax.experimental import pallas as pl
from jax.experimental.pallas import tpu as pltpu
from jax.sharding import PartitionSpec as P

blur_scale = 0.5
floor_value = -1e30
SLOTS = 3
CHUNK = 256


def tile_kernel(valid_ref, lhs_ref, bias_ref, rhs_ref, sub_ref, out_ref, acc_high, acc_total):
    outer = pl.program_id(0)
    inner = pl.program_id(1)
    n_inner = pl.num_programs(1)
    reduced = lhs_ref.shape[2]
    kept = rhs_ref.shape[2]

    @pl.when(inner == 0)
    def _():
        acc_high[...] = jnp.full((1, kept), floor_value, jnp.float32)
        acc_total[...] = jnp.zeros((1, kept), jnp.float32)

    @pl.when(valid_ref[outer * n_inner + inner] > 0)
    def _():
        rhs = rhs_ref[0]

        def chunk(ci, carry):
            high, total = carry
            start = pl.multiple_of(ci * CHUNK, CHUNK)
            left = lhs_ref[0, :, pl.ds(start, CHUNK)]
            vals = lax.dot_general(
                left, rhs, (((0,), (0,)), ((), ())), preferred_element_type=jnp.float32
            )
            bias_row = jnp.broadcast_to(bias_ref[0, :, pl.ds(start, CHUNK)], (8, CHUNK))
            vals = vals + jnp.transpose(bias_row)[:, 0:1]
            new_high = jnp.maximum(high, jnp.max(vals, axis=0, keepdims=True))
            total = total * jnp.exp(high - new_high) + jnp.sum(
                jnp.exp(vals - new_high), axis=0, keepdims=True
            )
            return new_high, total

        start = (
            jnp.full((1, kept), floor_value, jnp.float32),
            jnp.zeros((1, kept), jnp.float32),
        )
        high, total = lax.fori_loop(0, reduced // CHUNK, chunk, start, unroll=True)
        old_high = acc_high[...]
        new_high = jnp.maximum(old_high, high)
        acc_total[...] = acc_total[...] * jnp.exp(old_high - new_high) + total * jnp.exp(
            high - new_high
        )
        acc_high[...] = new_high

    @pl.when(inner == n_inner - 1)
    def _():
        total = acc_total[...]
        found = total > 0.0
        whole = acc_high[...] + jnp.log(jnp.where(found, total, 1.0))
        out_ref[0] = jnp.where(found, whole - sub_ref[0], floor_value)


def tile_lse(valid, lhs, bias, rhs, sub):
    n_in, depth, reduced = lhs.shape
    n_out, _, kept = rhs.shape
    grid_spec = pltpu.PrefetchScalarGridSpec(
        num_scalar_prefetch=1,
        grid=(n_out, n_in),
        in_specs=[
            pl.BlockSpec((1, depth, reduced), lambda o, n, v: (n, 0, 0)),
            pl.BlockSpec((1, 1, reduced), lambda o, n, v: (n, 0, 0)),
            pl.BlockSpec((1, depth, kept), lambda o, n, v: (o, 0, 0)),
            pl.BlockSpec((1, 1, kept), lambda o, n, v: (o, 0, 0)),
        ],
        out_specs=pl.BlockSpec((1, 1, kept), lambda o, n, v: (o, 0, 0)),
        scratch_shapes=[pltpu.VMEM((1, kept), jnp.float32), pltpu.VMEM((1, kept), jnp.float32)],
    )
    return pl.pallas_call(
        tile_kernel,
        grid_spec=grid_spec,
        out_shape=jax.ShapeDtypeStruct((n_out, 1, kept), jnp.float32),
    )(valid, lhs, bias, rhs, sub)


def masked_lse(values, mask, axis):
    high = jnp.max(jnp.where(mask, values, floor_value), axis=axis)
    total = jnp.sum(
        jnp.where(mask, jnp.exp(values - jnp.expand_dims(high, axis)), 0.0), axis=axis
    )
    return jnp.where(jnp.any(mask, axis=axis), high + jnp.log(total), floor_value)


def log_add(first, second):
    high = jnp.maximum(first, second)
    return high + jnp.log(jnp.exp(first - high) + jnp.exp(second - high))


def body(src_points, dst_points, support, log_src_mass, log_dst_mass, dst_potential, n_row, n_col):
    row_count, dim_part, pts = src_points.shape
    col_count = dst_points.shape[0]
    col_id = lax.axis_index("col")

    dst_copies = jnp.broadcast_to(dst_points[None], (n_row,) + dst_points.shape)
    dst_recv = lax.all_to_all(dst_copies, "row", 0, 0, tiled=True)

    dev_of = support // col_count
    touches = jnp.any(
        dev_of[:, :, None] == jnp.arange(n_col, dtype=jnp.int32)[None, None, :], axis=1
    )
    rank = jnp.cumsum(touches.astype(jnp.int32), axis=0) - 1
    onehot = touches.T[:, None, :] & (
        rank.T[:, None, :] == jnp.arange(SLOTS, dtype=jnp.int32)[None, :, None]
    )
    table = jnp.sum(
        onehot.astype(jnp.int32) * jnp.arange(row_count, dtype=jnp.int32)[None, None, :], axis=2
    )
    slot_ok = jnp.any(onehot, axis=2)

    send = jnp.take(src_points, table.reshape(-1), axis=0).reshape(
        n_col, SLOTS, dim_part, pts
    ) * 4
    dst_recv, send = lax.optimization_barrier((dst_recv, send))
    recv = lax.all_to_all(send, "col", 0, 0, tiled=True)
    src_four = recv.transpose(1, 0, 2, 3).reshape(SLOTS, n_col * dim_part, pts)

    dst_full = dst_recv.transpose(1, 0, 2, 3).reshape(col_count, -1, pts)
    my_table = lax.dynamic_index_in_dim(table, col_id, 0, keepdims=False)
    my_ok = lax.dynamic_index_in_dim(slot_ok, col_id, 0, keepdims=False)
    my_support = jnp.take(support, my_table, axis=0)
    valid = my_ok[:, None] & jnp.any(
        my_support[:, None, :]
        == (col_id * col_count + jnp.arange(col_count, dtype=jnp.int32))[None, :, None],
        axis=2,
    )

    src_vals = src_four.astype(jnp.float32)
    src_sq = jnp.sum(src_vals * src_vals, axis=1) / 16.0
    dst_vals = dst_full.astype(jnp.float32)
    dst_sq = jnp.sum(dst_vals * dst_vals, axis=1)

    valid_int = valid.astype(jnp.int32)
    dst_bias = (2.0 * dst_potential - 2.0 * dst_sq)[:, None, :]
    row_local = tile_lse(
        valid_int.reshape(-1), dst_full, dst_bias, src_four, (2.0 * src_sq)[:, None, :]
    )[:, 0, :]
    row_local = jnp.where(my_ok[:, None], row_local, floor_value)

    row_all = lax.all_gather(row_local, "col", axis=0, tiled=False)
    owner = onehot.transpose(2, 0, 1)
    whole = masked_lse(
        jnp.broadcast_to(row_all[None], (row_count, n_col, SLOTS, pts)).reshape(row_count, n_col * SLOTS, pts),
        owner.reshape(row_count, n_col * SLOTS)[:, :, None],
        axis=1,
    )
    src_new = blur_scale * (log_src_mass - whole)

    my_owner = jnp.take(owner, my_table, axis=0).reshape(SLOTS, n_col * SLOTS)
    my_whole = masked_lse(
        jnp.broadcast_to(row_all.reshape(1, n_col * SLOTS, pts), (SLOTS, n_col * SLOTS, pts)),
        my_owner[:, :, None],
        axis=1,
    )
    my_pot = blur_scale * (jnp.take(log_src_mass, my_table, axis=0) - my_whole)
    src_bias = (2.0 * my_pot - 2.0 * src_sq)[:, None, :]
    col_local = tile_lse(
        valid_int.T.reshape(-1), src_four, src_bias, dst_full, (2.0 * dst_sq)[:, None, :]
    )[:, 0, :]

    col_copies = jnp.broadcast_to(col_local[None], (n_row,) + col_local.shape)
    col_all = lax.all_to_all(col_copies, "row", 0, 0, tiled=True)
    col_high = jnp.max(col_all, axis=0)
    col_whole = col_high + jnp.log(jnp.sum(jnp.exp(col_all - col_high[None]), axis=0))
    dst_new = blur_scale * (log_dst_mass - col_whole)
    return (src_new, dst_new)


def solution(mesh):
    n_row = mesh.shape["row"]
    n_col = mesh.shape["col"]
    return jax.shard_map(
        functools.partial(body, n_row=n_row, n_col=n_col),
        mesh=mesh,
        in_specs=(
            P("row", "col", None),
            P("col", "row", None),
            P("row", None),
            P("row", None),
            P("col", None),
            P("col", None),
        ),
        out_specs=(P("row", None), P("col", None)),
        check_vma=False,
    )
```

```python
import functools

import jax
import jax.numpy as jnp
from jax import lax
from jax.experimental import pallas as pl
from jax.experimental.pallas import tpu as pltpu
from jax.sharding import PartitionSpec as P

blur_scale = 0.5
floor_value = -1e30
SLOTS = 3
CHUNK = 256


def tile_kernel(valid_ref, lhs_ref, bias_ref, rhs_ref, sub_ref, out_ref, acc_high, acc_total):
    outer = pl.program_id(0)
    inner = pl.program_id(1)
    n_inner = pl.num_programs(1)
    reduced = lhs_ref.shape[2]
    kept = rhs_ref.shape[2]

    @pl.when(inner == 0)
    def _():
        acc_high[...] = jnp.full((1, kept), floor_value, jnp.float32)
        acc_total[...] = jnp.zeros((1, kept), jnp.float32)

    @pl.when(valid_ref[outer * n_inner + inner] > 0)
    def _():
        rhs = rhs_ref[0]

        def chunk(ci, carry):
            high, total = carry
            start = pl.multiple_of(ci * CHUNK, CHUNK)
            left = lhs_ref[0, :, pl.ds(start, CHUNK)]
            vals = lax.dot_general(
                left, rhs, (((0,), (0,)), ((), ())), preferred_element_type=jnp.float32
            )
            vals = vals + bias_ref[0, pl.ds(start, CHUNK), :]
            new_high = jnp.maximum(high, jnp.max(vals, axis=0, keepdims=True))
            total = total * jnp.exp(high - new_high) + jnp.sum(
                jnp.exp(vals - new_high), axis=0, keepdims=True
            )
            return new_high, total

        start = (
            jnp.full((1, kept), floor_value, jnp.float32),
            jnp.zeros((1, kept), jnp.float32),
        )
        high, total = lax.fori_loop(0, reduced // CHUNK, chunk, start, unroll=True)
        old_high = acc_high[...]
        new_high = jnp.maximum(old_high, high)
        acc_total[...] = acc_total[...] * jnp.exp(old_high - new_high) + total * jnp.exp(
            high - new_high
        )
        acc_high[...] = new_high

    @pl.when(inner == n_inner - 1)
    def _():
        total = acc_total[...]
        found = total > 0.0
        whole = acc_high[...] + jnp.log(jnp.where(found, total, 1.0))
        out_ref[0] = jnp.where(found, whole - sub_ref[0], floor_value)


def tile_lse(valid, lhs, bias, rhs, sub):
    n_in, depth, reduced = lhs.shape
    n_out, _, kept = rhs.shape
    grid_spec = pltpu.PrefetchScalarGridSpec(
        num_scalar_prefetch=1,
        grid=(n_out, n_in),
        in_specs=[
            pl.BlockSpec((1, depth, reduced), lambda o, n, v: (n, 0, 0)),
            pl.BlockSpec((1, reduced, 1), lambda o, n, v: (n, 0, 0)),
            pl.BlockSpec((1, depth, kept), lambda o, n, v: (o, 0, 0)),
            pl.BlockSpec((1, 1, kept), lambda o, n, v: (o, 0, 0)),
        ],
        out_specs=pl.BlockSpec((1, 1, kept), lambda o, n, v: (o, 0, 0)),
        scratch_shapes=[pltpu.VMEM((1, kept), jnp.float32), pltpu.VMEM((1, kept), jnp.float32)],
    )
    return pl.pallas_call(
        tile_kernel,
        grid_spec=grid_spec,
        out_shape=jax.ShapeDtypeStruct((n_out, 1, kept), jnp.float32),
    )(valid, lhs, bias, rhs, sub)


def masked_lse(values, mask, axis):
    high = jnp.max(jnp.where(mask, values, floor_value), axis=axis)
    total = jnp.sum(
        jnp.where(mask, jnp.exp(values - jnp.expand_dims(high, axis)), 0.0), axis=axis
    )
    return jnp.where(jnp.any(mask, axis=axis), high + jnp.log(total), floor_value)


def log_add(first, second):
    high = jnp.maximum(first, second)
    return high + jnp.log(jnp.exp(first - high) + jnp.exp(second - high))


def body(src_points, dst_points, support, log_src_mass, log_dst_mass, dst_potential, n_row, n_col):
    row_count, dim_part, pts = src_points.shape
    col_count = dst_points.shape[0]
    col_id = lax.axis_index("col")

    dst_copies = jnp.broadcast_to(dst_points[None], (n_row,) + dst_points.shape)
    dst_recv = lax.all_to_all(dst_copies, "row", 0, 0, tiled=True)

    dev_of = support // col_count
    touches = jnp.any(
        dev_of[:, :, None] == jnp.arange(n_col, dtype=jnp.int32)[None, None, :], axis=1
    )
    rank = jnp.cumsum(touches.astype(jnp.int32), axis=0) - 1
    onehot = touches.T[:, None, :] & (
        rank.T[:, None, :] == jnp.arange(SLOTS, dtype=jnp.int32)[None, :, None]
    )
    table = jnp.sum(
        onehot.astype(jnp.int32) * jnp.arange(row_count, dtype=jnp.int32)[None, None, :], axis=2
    )
    slot_ok = jnp.any(onehot, axis=2)

    send = jnp.take(src_points, table.reshape(-1), axis=0).reshape(
        n_col, SLOTS, dim_part, pts
    ) * 4
    dst_recv, send = lax.optimization_barrier((dst_recv, send))
    recv = lax.all_to_all(send, "col", 0, 0, tiled=True)
    src_four = recv.transpose(1, 0, 2, 3).reshape(SLOTS, n_col * dim_part, pts)

    dst_full = dst_recv.transpose(1, 0, 2, 3).reshape(col_count, -1, pts)
    my_table = lax.dynamic_index_in_dim(table, col_id, 0, keepdims=False)
    my_ok = lax.dynamic_index_in_dim(slot_ok, col_id, 0, keepdims=False)
    my_support = jnp.take(support, my_table, axis=0)
    valid = my_ok[:, None] & jnp.any(
        my_support[:, None, :]
        == (col_id * col_count + jnp.arange(col_count, dtype=jnp.int32))[None, :, None],
        axis=2,
    )

    src_vals = src_four.astype(jnp.float32)
    src_sq = jnp.sum(src_vals * src_vals, axis=1) / 16.0
    dst_vals = dst_full.astype(jnp.float32)
    dst_sq = jnp.sum(dst_vals * dst_vals, axis=1)

    valid_int = valid.astype(jnp.int32)
    dst_bias = (2.0 * dst_potential - 2.0 * dst_sq)[:, :, None]
    row_local = tile_lse(
        valid_int.reshape(-1), dst_full, dst_bias, src_four, (2.0 * src_sq)[:, None, :]
    )[:, 0, :]
    row_local = jnp.where(my_ok[:, None], row_local, floor_value)

    row_all = lax.all_gather(row_local, "col", axis=0, tiled=False)
    owner = onehot.transpose(2, 0, 1)
    whole = masked_lse(
        jnp.broadcast_to(row_all[None], (row_count, n_col, SLOTS, pts)).reshape(row_count, n_col * SLOTS, pts),
        owner.reshape(row_count, n_col * SLOTS)[:, :, None],
        axis=1,
    )
    src_new = blur_scale * (log_src_mass - whole)

    my_owner = jnp.take(owner, my_table, axis=0).reshape(SLOTS, n_col * SLOTS)
    my_whole = masked_lse(
        jnp.broadcast_to(row_all.reshape(1, n_col * SLOTS, pts), (SLOTS, n_col * SLOTS, pts)),
        my_owner[:, :, None],
        axis=1,
    )
    my_pot = blur_scale * (jnp.take(log_src_mass, my_table, axis=0) - my_whole)
    src_bias = (2.0 * my_pot - 2.0 * src_sq)[:, :, None]
    col_local = tile_lse(
        valid_int.T.reshape(-1), src_four, src_bias, dst_full, (2.0 * dst_sq)[:, None, :]
    )[:, 0, :]

    col_copies = jnp.broadcast_to(col_local[None], (n_row,) + col_local.shape)
    col_all = lax.all_to_all(col_copies, "row", 0, 0, tiled=True)
    col_high = jnp.max(col_all, axis=0)
    col_whole = col_high + jnp.log(jnp.sum(jnp.exp(col_all - col_high[None]), axis=0))
    dst_new = blur_scale * (log_dst_mass - col_whole)
    return (src_new, dst_new)


def solution(mesh):
    n_row = mesh.shape["row"]
    n_col = mesh.shape["col"]
    return jax.shard_map(
        functools.partial(body, n_row=n_row, n_col=n_col),
        mesh=mesh,
        in_specs=(
            P("row", "col", None),
            P("col", "row", None),
            P("row", None),
            P("row", None),
            P("col", None),
            P("col", None),
        ),
        out_specs=(P("row", None), P("col", None)),
        check_vma=False,
    )
```

```python
import functools

import jax
import jax.numpy as jnp
from jax import lax
from jax.experimental import pallas as pl
from jax.experimental.pallas import tpu as pltpu
from jax.sharding import PartitionSpec as P

blur_scale = 0.5
floor_value = -1e30
SLOTS = 3
CHUNK = 256


def tile_kernel(valid_ref, lhs_ref, bias_ref, rhs_ref, sub_ref, out_ref, acc_high, acc_total):
    outer = pl.program_id(0)
    inner = pl.program_id(1)
    n_inner = pl.num_programs(1)
    reduced = lhs_ref.shape[2]
    kept = rhs_ref.shape[2]

    @pl.when(inner == 0)
    def _():
        acc_high[...] = jnp.full((1, kept), floor_value, jnp.float32)
        acc_total[...] = jnp.zeros((1, kept), jnp.float32)

    @pl.when(valid_ref[outer * n_inner + inner] > 0)
    def _():
        rhs = rhs_ref[0]

        def chunk(ci, carry):
            high, total = carry
            start = pl.multiple_of(ci * CHUNK, CHUNK)
            left = lhs_ref[0, :, pl.ds(start, CHUNK)]
            vals = lax.dot_general(
                left, rhs, (((0,), (0,)), ((), ())), preferred_element_type=jnp.float32
            )
            vals = vals + bias_ref[0, pl.ds(start, CHUNK), :]
            new_high = jnp.maximum(high, jnp.max(vals, axis=0, keepdims=True))
            total = total * jnp.exp(high - new_high) + jnp.sum(
                jnp.exp(vals - new_high), axis=0, keepdims=True
            )
            return new_high, total

        start = (
            jnp.full((1, kept), floor_value, jnp.float32),
            jnp.zeros((1, kept), jnp.float32),
        )
        high, total = lax.fori_loop(0, reduced // CHUNK, chunk, start, unroll=True)
        old_high = acc_high[...]
        new_high = jnp.maximum(old_high, high)
        acc_total[...] = acc_total[...] * jnp.exp(old_high - new_high) + total * jnp.exp(
            high - new_high
        )
        acc_high[...] = new_high

    @pl.when(inner == n_inner - 1)
    def _():
        total = acc_total[...]
        found = total > 0.0
        whole = acc_high[...] + jnp.log(jnp.where(found, total, 1.0))
        out_ref[0] = jnp.where(found, whole - sub_ref[0], floor_value)


def tile_lse(valid, lhs, bias, rhs, sub):
    n_in, depth, reduced = lhs.shape
    n_out, _, kept = rhs.shape
    grid_spec = pltpu.PrefetchScalarGridSpec(
        num_scalar_prefetch=1,
        grid=(n_out, n_in),
        in_specs=[
            pl.BlockSpec((1, depth, reduced), lambda o, n, v: (n, 0, 0)),
            pl.BlockSpec((1, reduced, 1), lambda o, n, v: (n, 0, 0)),
            pl.BlockSpec((1, depth, kept), lambda o, n, v: (o, 0, 0)),
            pl.BlockSpec((1, 1, kept), lambda o, n, v: (o, 0, 0)),
        ],
        out_specs=pl.BlockSpec((1, 1, kept), lambda o, n, v: (o, 0, 0)),
        scratch_shapes=[pltpu.VMEM((1, kept), jnp.float32), pltpu.VMEM((1, kept), jnp.float32)],
    )
    return pl.pallas_call(
        tile_kernel,
        grid_spec=grid_spec,
        out_shape=jax.ShapeDtypeStruct((n_out, 1, kept), jnp.float32),
    )(valid, lhs, bias, rhs, sub)


def masked_lse(values, mask, axis):
    high = jnp.max(jnp.where(mask, values, floor_value), axis=axis)
    total = jnp.sum(
        jnp.where(mask, jnp.exp(values - jnp.expand_dims(high, axis)), 0.0), axis=axis
    )
    return jnp.where(jnp.any(mask, axis=axis), high + jnp.log(total), floor_value)


def log_add(first, second):
    high = jnp.maximum(first, second)
    return high + jnp.log(jnp.exp(first - high) + jnp.exp(second - high))


def body(src_points, dst_points, support, log_src_mass, log_dst_mass, dst_potential, n_row, n_col):
    row_count, dim_part, pts = src_points.shape
    col_count = dst_points.shape[0]
    col_id = lax.axis_index("col")

    dst_copies = jnp.broadcast_to(dst_points[None], (n_row,) + dst_points.shape)
    dst_recv = lax.all_to_all(dst_copies, "row", 0, 0, tiled=True)

    dev_of = support // col_count
    touches = jnp.any(
        dev_of[:, :, None] == jnp.arange(n_col, dtype=jnp.int32)[None, None, :], axis=1
    )
    rank = jnp.cumsum(touches.astype(jnp.int32), axis=0) - 1
    onehot = touches.T[:, None, :] & (
        rank.T[:, None, :] == jnp.arange(SLOTS, dtype=jnp.int32)[None, :, None]
    )
    table = jnp.sum(
        onehot.astype(jnp.int32) * jnp.arange(row_count, dtype=jnp.int32)[None, None, :], axis=2
    )
    slot_ok = jnp.any(onehot, axis=2)

    send = jnp.take(src_points, table.reshape(-1), axis=0).reshape(
        n_col, SLOTS, dim_part, pts
    ) * 4
    dst_recv, send = lax.optimization_barrier((dst_recv, send))
    recv = lax.all_to_all(send, "col", 0, 0, tiled=True)
    src_four = recv.transpose(1, 0, 2, 3).reshape(SLOTS, n_col * dim_part, pts)

    dst_full = dst_recv.transpose(1, 0, 2, 3).reshape(col_count, -1, pts)
    my_table = lax.dynamic_index_in_dim(table, col_id, 0, keepdims=False)
    my_ok = lax.dynamic_index_in_dim(slot_ok, col_id, 0, keepdims=False)
    my_support = jnp.take(support, my_table, axis=0)
    valid = my_ok[:, None] & jnp.any(
        my_support[:, None, :]
        == (col_id * col_count + jnp.arange(col_count, dtype=jnp.int32))[None, :, None],
        axis=2,
    )

    src_vals = src_four.astype(jnp.float32)
    src_sq = jnp.sum(src_vals * src_vals, axis=1) / 16.0
    dst_vals = dst_full.astype(jnp.float32)
    dst_sq = jnp.sum(dst_vals * dst_vals, axis=1)

    valid_int = valid.astype(jnp.int32)
    dst_bias = (2.0 * dst_potential - 2.0 * dst_sq)[:, :, None]
    row_local = tile_lse(
        valid_int.reshape(-1), dst_full, dst_bias, src_four, (2.0 * src_sq)[:, None, :]
    )[:, 0, :]
    row_local = jnp.where(my_ok[:, None], row_local, floor_value)

    row_all = lax.all_gather(row_local, "col", axis=0, tiled=False)
    owner = onehot.transpose(2, 0, 1)
    whole = masked_lse(
        jnp.broadcast_to(row_all[None], (row_count, n_col, SLOTS, pts)).reshape(row_count, n_col * SLOTS, pts),
        owner.reshape(row_count, n_col * SLOTS)[:, :, None],
        axis=1,
    )
    src_new = blur_scale * (log_src_mass - whole)

    my_owner = jnp.take(owner, my_table, axis=0).reshape(SLOTS, n_col * SLOTS)
    my_whole = masked_lse(
        jnp.broadcast_to(row_all.reshape(1, n_col * SLOTS, pts), (SLOTS, n_col * SLOTS, pts)),
        my_owner[:, :, None],
        axis=1,
    )
    my_pot = blur_scale * (jnp.take(log_src_mass, my_table, axis=0) - my_whole)
    src_bias = (2.0 * my_pot - 2.0 * src_sq)[:, :, None]
    src_new, src_bias = lax.optimization_barrier((src_new, src_bias))
    col_local = tile_lse(
        valid_int.T.reshape(-1), src_four, src_bias, dst_full, (2.0 * dst_sq)[:, None, :]
    )[:, 0, :]

    col_copies = jnp.broadcast_to(col_local[None], (n_row,) + col_local.shape)
    col_all = lax.all_to_all(col_copies, "row", 0, 0, tiled=True)
    col_high = jnp.max(col_all, axis=0)
    col_whole = col_high + jnp.log(jnp.sum(jnp.exp(col_all - col_high[None]), axis=0))
    dst_new = blur_scale * (log_dst_mass - col_whole)
    return (src_new, dst_new)


def solution(mesh):
    n_row = mesh.shape["row"]
    n_col = mesh.shape["col"]
    return jax.shard_map(
        functools.partial(body, n_row=n_row, n_col=n_col),
        mesh=mesh,
        in_specs=(
            P("row", "col", None),
            P("col", "row", None),
            P("row", None),
            P("row", None),
            P("col", None),
            P("col", None),
        ),
        out_specs=(P("row", None), P("col", None)),
        check_vma=False,
    )
```

```python
import functools

import jax
import jax.numpy as jnp
from jax import lax
from jax.experimental import pallas as pl
from jax.experimental.pallas import tpu as pltpu
from jax.sharding import PartitionSpec as P

blur_scale = 0.5
floor_value = -1e30
SLOTS = 3
CHUNK = 256


def tile_kernel(valid_ref, lhs_ref, bias_ref, rhs_ref, sub_ref, out_ref, acc_high, acc_total):
    outer = pl.program_id(0)
    inner = pl.program_id(1)
    n_inner = pl.num_programs(1)
    reduced = lhs_ref.shape[2]
    kept = rhs_ref.shape[2]

    @pl.when(inner == 0)
    def _():
        acc_high[...] = jnp.full((1, kept), floor_value, jnp.float32)
        acc_total[...] = jnp.zeros((1, kept), jnp.float32)

    @pl.when(valid_ref[outer * n_inner + inner] > 0)
    def _():
        rhs = rhs_ref[0]

        def chunk(ci, carry):
            high, total = carry
            start = pl.multiple_of(ci * CHUNK, CHUNK)
            left = lhs_ref[0, :, pl.ds(start, CHUNK)]
            vals = lax.dot_general(
                left, rhs, (((0,), (0,)), ((), ())), preferred_element_type=jnp.float32
            )
            vals = vals + bias_ref[0, pl.ds(start, CHUNK), :]
            new_high = jnp.maximum(high, jnp.max(vals, axis=0, keepdims=True))
            total = total * jnp.exp(high - new_high) + jnp.sum(
                jnp.exp(vals - new_high), axis=0, keepdims=True
            )
            return new_high, total

        start = (
            jnp.full((1, kept), floor_value, jnp.float32),
            jnp.zeros((1, kept), jnp.float32),
        )
        high, total = lax.fori_loop(0, reduced // CHUNK, chunk, start, unroll=True)
        old_high = acc_high[...]
        new_high = jnp.maximum(old_high, high)
        acc_total[...] = acc_total[...] * jnp.exp(old_high - new_high) + total * jnp.exp(
            high - new_high
        )
        acc_high[...] = new_high

    @pl.when(inner == n_inner - 1)
    def _():
        total = acc_total[...]
        found = total > 0.0
        whole = acc_high[...] + jnp.log(jnp.where(found, total, 1.0))
        out_ref[0] = jnp.where(found, whole - sub_ref[0], floor_value)


def tile_lse(valid, lhs, bias, rhs, sub):
    n_in, depth, reduced = lhs.shape
    n_out, _, kept = rhs.shape
    grid_spec = pltpu.PrefetchScalarGridSpec(
        num_scalar_prefetch=1,
        grid=(n_out, n_in),
        in_specs=[
            pl.BlockSpec((1, depth, reduced), lambda o, n, v: (n, 0, 0)),
            pl.BlockSpec((1, reduced, 1), lambda o, n, v: (n, 0, 0)),
            pl.BlockSpec((1, depth, kept), lambda o, n, v: (o, 0, 0)),
            pl.BlockSpec((1, 1, kept), lambda o, n, v: (o, 0, 0)),
        ],
        out_specs=pl.BlockSpec((1, 1, kept), lambda o, n, v: (o, 0, 0)),
        scratch_shapes=[pltpu.VMEM((1, kept), jnp.float32), pltpu.VMEM((1, kept), jnp.float32)],
    )
    return pl.pallas_call(
        tile_kernel,
        grid_spec=grid_spec,
        out_shape=jax.ShapeDtypeStruct((n_out, 1, kept), jnp.float32),
    )(valid, lhs, bias, rhs, sub)


def masked_lse(values, mask, axis):
    high = jnp.max(jnp.where(mask, values, floor_value), axis=axis)
    total = jnp.sum(
        jnp.where(mask, jnp.exp(values - jnp.expand_dims(high, axis)), 0.0), axis=axis
    )
    return jnp.where(jnp.any(mask, axis=axis), high + jnp.log(total), floor_value)


def log_add(first, second):
    high = jnp.maximum(first, second)
    return high + jnp.log(jnp.exp(first - high) + jnp.exp(second - high))


def body(src_points, dst_points, support, log_src_mass, log_dst_mass, dst_potential, n_row, n_col):
    row_count, dim_part, pts = src_points.shape
    col_count = dst_points.shape[0]
    col_id = lax.axis_index("col")

    dst_copies = jnp.broadcast_to(dst_points[None], (n_row,) + dst_points.shape)
    dst_recv = lax.all_to_all(dst_copies, "row", 0, 0, tiled=True)

    dev_of = support // col_count
    touches = jnp.any(
        dev_of[:, :, None] == jnp.arange(n_col, dtype=jnp.int32)[None, None, :], axis=1
    )
    rank = jnp.cumsum(touches.astype(jnp.int32), axis=0) - 1
    onehot = touches.T[:, None, :] & (
        rank.T[:, None, :] == jnp.arange(SLOTS, dtype=jnp.int32)[None, :, None]
    )
    table = jnp.sum(
        onehot.astype(jnp.int32) * jnp.arange(row_count, dtype=jnp.int32)[None, None, :], axis=2
    )
    slot_ok = jnp.any(onehot, axis=2)

    send = jnp.take(src_points, table.reshape(-1), axis=0).reshape(
        n_col, SLOTS, dim_part, pts
    ) * 4
    dst_recv, send = lax.optimization_barrier((dst_recv, send))
    recv = lax.all_to_all(send, "col", 0, 0, tiled=True)
    src_four = recv.transpose(1, 0, 2, 3).reshape(SLOTS, n_col * dim_part, pts)

    dst_full = dst_recv.transpose(1, 0, 2, 3).reshape(col_count, -1, pts)
    my_table = lax.dynamic_index_in_dim(table, col_id, 0, keepdims=False)
    my_ok = lax.dynamic_index_in_dim(slot_ok, col_id, 0, keepdims=False)
    my_support = jnp.take(support, my_table, axis=0)
    valid = my_ok[:, None] & jnp.any(
        my_support[:, None, :]
        == (col_id * col_count + jnp.arange(col_count, dtype=jnp.int32))[None, :, None],
        axis=2,
    )

    src_vals = src_four.astype(jnp.float32)
    src_sq = jnp.sum(src_vals * src_vals, axis=1) / 16.0
    dst_vals = dst_full.astype(jnp.float32)
    dst_sq = jnp.sum(dst_vals * dst_vals, axis=1)

    valid_int = valid.astype(jnp.int32)
    dst_bias = (2.0 * dst_potential - 2.0 * dst_sq)[:, :, None]
    row_local = tile_lse(
        valid_int.reshape(-1), dst_full, dst_bias, src_four, (2.0 * src_sq)[:, None, :]
    )[:, 0, :]
    row_local = jnp.where(my_ok[:, None], row_local, floor_value)

    row_all = lax.all_gather(row_local, "col", axis=0, tiled=False)
    owner = onehot.transpose(2, 0, 1)
    whole = masked_lse(
        jnp.broadcast_to(row_all[None], (row_count, n_col, SLOTS, pts)).reshape(row_count, n_col * SLOTS, pts),
        owner.reshape(row_count, n_col * SLOTS)[:, :, None],
        axis=1,
    )
    src_new = blur_scale * (log_src_mass - whole)

    my_pot = jnp.take(src_new, my_table, axis=0)
    src_bias = (2.0 * my_pot - 2.0 * src_sq)[:, :, None]
    col_local = tile_lse(
        valid_int.T.reshape(-1), src_four, src_bias, dst_full, (2.0 * dst_sq)[:, None, :]
    )[:, 0, :]

    col_all = lax.all_gather(col_local, "row", axis=0, tiled=False)
    col_high = jnp.max(col_all, axis=0)
    col_whole = col_high + jnp.log(jnp.sum(jnp.exp(col_all - col_high[None]), axis=0))
    dst_new = blur_scale * (log_dst_mass - col_whole)
    return (src_new, dst_new)


def solution(mesh):
    n_row = mesh.shape["row"]
    n_col = mesh.shape["col"]
    return jax.shard_map(
        functools.partial(body, n_row=n_row, n_col=n_col),
        mesh=mesh,
        in_specs=(
            P("row", "col", None),
            P("col", "row", None),
            P("row", None),
            P("row", None),
            P("col", None),
            P("col", None),
        ),
        out_specs=(P("row", None), P("col", None)),
        check_vma=False,
    )
```

```python
import functools

import jax
import jax.numpy as jnp
from jax import lax
from jax.experimental import pallas as pl
from jax.experimental.pallas import tpu as pltpu
from jax.sharding import PartitionSpec as P

blur_scale = 0.5
floor_value = -1e30
SLOTS = 3
CHUNK = 256


def tile_kernel(valid_ref, lhs_ref, bias_ref, rhs_ref, sub_ref, out_ref, acc_high, acc_total):
    outer = pl.program_id(0)
    inner = pl.program_id(1)
    n_inner = pl.num_programs(1)
    reduced = lhs_ref.shape[2]
    kept = rhs_ref.shape[2]

    @pl.when(inner == 0)
    def _():
        acc_high[...] = jnp.full((1, kept), floor_value, jnp.float32)
        acc_total[...] = jnp.zeros((1, kept), jnp.float32)

    @pl.when(valid_ref[outer * n_inner + inner] > 0)
    def _():
        rhs = rhs_ref[0]

        def chunk(ci, carry):
            high, total = carry
            start = pl.multiple_of(ci * CHUNK, CHUNK)
            left = lhs_ref[0, :, pl.ds(start, CHUNK)]
            vals = lax.dot_general(
                left, rhs, (((0,), (0,)), ((), ())), preferred_element_type=jnp.float32
            )
            vals = vals + bias_ref[0, pl.ds(start, CHUNK), :]
            new_high = jnp.maximum(high, jnp.max(vals, axis=0, keepdims=True))
            total = total * jnp.exp(high - new_high) + jnp.sum(
                jnp.exp(vals - new_high), axis=0, keepdims=True
            )
            return new_high, total

        start = (
            jnp.full((1, kept), floor_value, jnp.float32),
            jnp.zeros((1, kept), jnp.float32),
        )
        high, total = lax.fori_loop(0, reduced // CHUNK, chunk, start, unroll=True)
        old_high = acc_high[...]
        new_high = jnp.maximum(old_high, high)
        acc_total[...] = acc_total[...] * jnp.exp(old_high - new_high) + total * jnp.exp(
            high - new_high
        )
        acc_high[...] = new_high

    @pl.when(inner == n_inner - 1)
    def _():
        total = acc_total[...]
        found = total > 0.0
        whole = acc_high[...] + jnp.log(jnp.where(found, total, 1.0))
        out_ref[0] = jnp.where(found, whole - sub_ref[0], floor_value)


def tile_lse(valid, lhs, bias, rhs, sub):
    n_in, depth, reduced = lhs.shape
    n_out, _, kept = rhs.shape
    grid_spec = pltpu.PrefetchScalarGridSpec(
        num_scalar_prefetch=1,
        grid=(n_out, n_in),
        in_specs=[
            pl.BlockSpec((1, depth, reduced), lambda o, n, v: (n, 0, 0)),
            pl.BlockSpec((1, reduced, 1), lambda o, n, v: (n, 0, 0)),
            pl.BlockSpec((1, depth, kept), lambda o, n, v: (o, 0, 0)),
            pl.BlockSpec((1, 1, kept), lambda o, n, v: (o, 0, 0)),
        ],
        out_specs=pl.BlockSpec((1, 1, kept), lambda o, n, v: (o, 0, 0)),
        scratch_shapes=[pltpu.VMEM((1, kept), jnp.float32), pltpu.VMEM((1, kept), jnp.float32)],
    )
    return pl.pallas_call(
        tile_kernel,
        grid_spec=grid_spec,
        out_shape=jax.ShapeDtypeStruct((n_out, 1, kept), jnp.float32),
    )(valid, lhs, bias, rhs, sub)


def masked_lse(values, mask, axis):
    high = jnp.max(jnp.where(mask, values, floor_value), axis=axis)
    total = jnp.sum(
        jnp.where(mask, jnp.exp(values - jnp.expand_dims(high, axis)), 0.0), axis=axis
    )
    return jnp.where(jnp.any(mask, axis=axis), high + jnp.log(total), floor_value)


def log_add(first, second):
    high = jnp.maximum(first, second)
    return high + jnp.log(jnp.exp(first - high) + jnp.exp(second - high))


def body(src_points, dst_points, support, log_src_mass, log_dst_mass, dst_potential, n_row, n_col):
    row_count, dim_part, pts = src_points.shape
    col_count = dst_points.shape[0]
    col_id = lax.axis_index("col")

    dst_copies = jnp.broadcast_to(dst_points[None], (n_row,) + dst_points.shape)
    dst_recv = lax.all_to_all(dst_copies, "row", 0, 0, tiled=True)

    dev_of = support // col_count
    touches = jnp.any(
        dev_of[:, :, None] == jnp.arange(n_col, dtype=jnp.int32)[None, None, :], axis=1
    )
    rank = jnp.cumsum(touches.astype(jnp.int32), axis=0) - 1
    onehot = touches.T[:, None, :] & (
        rank.T[:, None, :] == jnp.arange(SLOTS, dtype=jnp.int32)[None, :, None]
    )
    table = jnp.sum(
        onehot.astype(jnp.int32) * jnp.arange(row_count, dtype=jnp.int32)[None, None, :], axis=2
    )
    slot_ok = jnp.any(onehot, axis=2)

    send = jnp.take(src_points, table.reshape(-1), axis=0).reshape(
        n_col, SLOTS, dim_part, pts
    ) * 4
    dst_recv, send = lax.optimization_barrier((dst_recv, send))
    recv = lax.all_to_all(send, "col", 0, 0, tiled=True)
    src_four = recv.transpose(1, 0, 2, 3).reshape(SLOTS, n_col * dim_part, pts)

    dst_full = dst_recv.transpose(1, 0, 2, 3).reshape(col_count, -1, pts)
    my_table = lax.dynamic_index_in_dim(table, col_id, 0, keepdims=False)
    my_ok = lax.dynamic_index_in_dim(slot_ok, col_id, 0, keepdims=False)
    my_support = jnp.take(support, my_table, axis=0)
    valid = my_ok[:, None] & jnp.any(
        my_support[:, None, :]
        == (col_id * col_count + jnp.arange(col_count, dtype=jnp.int32))[None, :, None],
        axis=2,
    )

    src_vals = src_four.astype(jnp.float32)
    src_sq = jnp.sum(src_vals * src_vals, axis=1) / 16.0
    dst_vals = dst_full.astype(jnp.float32)
    dst_sq = jnp.sum(dst_vals * dst_vals, axis=1)

    valid_int = valid.astype(jnp.int32)
    dst_bias = (2.0 * dst_potential - 2.0 * dst_sq)[:, :, None]
    row_local = tile_lse(
        valid_int.reshape(-1), dst_full, dst_bias, src_four, (2.0 * src_sq)[:, None, :]
    )[:, 0, :]

    row_all = lax.all_gather(row_local, "col", axis=0, tiled=False)
    owner = onehot.transpose(2, 0, 1)
    whole = masked_lse(
        jnp.broadcast_to(row_all[None], (row_count, n_col, SLOTS, pts)).reshape(row_count, n_col * SLOTS, pts),
        owner.reshape(row_count, n_col * SLOTS)[:, :, None],
        axis=1,
    )
    src_new = blur_scale * (log_src_mass - whole)

    my_pot = jnp.take(src_new, my_table, axis=0)
    src_bias = (2.0 * my_pot - 2.0 * src_sq)[:, :, None]
    col_local = tile_lse(
        valid_int.T.reshape(-1), src_four, src_bias, dst_full, (2.0 * dst_sq)[:, None, :]
    )[:, 0, :]

    col_copies = jnp.broadcast_to(col_local[None], (n_row,) + col_local.shape)
    col_all = lax.all_to_all(col_copies, "row", 0, 0, tiled=True)
    col_high = jnp.max(col_all, axis=0)
    col_whole = col_high + jnp.log(jnp.sum(jnp.exp(col_all - col_high[None]), axis=0))
    dst_new = blur_scale * (log_dst_mass - col_whole)
    return (src_new, dst_new)


def solution(mesh):
    n_row = mesh.shape["row"]
    n_col = mesh.shape["col"]
    return jax.shard_map(
        functools.partial(body, n_row=n_row, n_col=n_col),
        mesh=mesh,
        in_specs=(
            P("row", "col", None),
            P("col", "row", None),
            P("row", None),
            P("row", None),
            P("col", None),
            P("col", None),
        ),
        out_specs=(P("row", None), P("col", None)),
        check_vma=False,
    )
```

```python
import functools

import jax
import jax.numpy as jnp
from jax import lax
from jax.experimental import pallas as pl
from jax.experimental.pallas import tpu as pltpu
from jax.sharding import PartitionSpec as P

blur_scale = 0.5
floor_value = -1e30
SLOTS = 3
CHUNK = 256


def tile_kernel(valid_ref, lhs_ref, bias_ref, rhs_ref, sub_ref, out_ref, acc_high, acc_total, dense_bias):
    outer = pl.program_id(0)
    inner = pl.program_id(1)
    n_inner = pl.num_programs(1)
    reduced = lhs_ref.shape[2]
    kept = rhs_ref.shape[2]

    @pl.when(inner == 0)
    def _():
        acc_high[...] = jnp.full((1, kept), floor_value, jnp.float32)
        acc_total[...] = jnp.zeros((1, kept), jnp.float32)

    @pl.when(valid_ref[outer * n_inner + inner] > 0)
    def _():
        rhs = rhs_ref[0]

        def chunk(ci, carry):
            high, total = carry
            start = pl.multiple_of(ci * CHUNK, CHUNK)
            left = lhs_ref[0, :, pl.ds(start, CHUNK)]
            vals = lax.dot_general(
                left, rhs, (((0,), (0,)), ((), ())), preferred_element_type=jnp.float32
            )
            if dense_bias:
                bias_row = jnp.broadcast_to(bias_ref[0, :, pl.ds(start, CHUNK)], (8, CHUNK))
                vals = vals + jnp.transpose(bias_row)[:, 0:1]
            else:
                vals = vals + bias_ref[0, pl.ds(start, CHUNK), :]
            new_high = jnp.maximum(high, jnp.max(vals, axis=0, keepdims=True))
            total = total * jnp.exp(high - new_high) + jnp.sum(
                jnp.exp(vals - new_high), axis=0, keepdims=True
            )
            return new_high, total

        start = (
            jnp.full((1, kept), floor_value, jnp.float32),
            jnp.zeros((1, kept), jnp.float32),
        )
        high, total = lax.fori_loop(0, reduced // CHUNK, chunk, start, unroll=True)
        old_high = acc_high[...]
        new_high = jnp.maximum(old_high, high)
        acc_total[...] = acc_total[...] * jnp.exp(old_high - new_high) + total * jnp.exp(
            high - new_high
        )
        acc_high[...] = new_high

    @pl.when(inner == n_inner - 1)
    def _():
        total = acc_total[...]
        found = total > 0.0
        whole = acc_high[...] + jnp.log(jnp.where(found, total, 1.0))
        out_ref[0] = jnp.where(found, whole - sub_ref[0], floor_value)


def tile_lse(valid, lhs, bias, rhs, sub, dense_bias=False):
    n_in, depth, reduced = lhs.shape
    n_out, _, kept = rhs.shape
    grid_spec = pltpu.PrefetchScalarGridSpec(
        num_scalar_prefetch=1,
        grid=(n_out, n_in),
        in_specs=[
            pl.BlockSpec((1, depth, reduced), lambda o, n, v: (n, 0, 0)),
            pl.BlockSpec((1,) + bias.shape[1:], lambda o, n, v: (n, 0, 0)),
            pl.BlockSpec((1, depth, kept), lambda o, n, v: (o, 0, 0)),
            pl.BlockSpec((1, 1, kept), lambda o, n, v: (o, 0, 0)),
        ],
        out_specs=pl.BlockSpec((1, 1, kept), lambda o, n, v: (o, 0, 0)),
        scratch_shapes=[pltpu.VMEM((1, kept), jnp.float32), pltpu.VMEM((1, kept), jnp.float32)],
    )
    return pl.pallas_call(
        functools.partial(tile_kernel, dense_bias=dense_bias),
        grid_spec=grid_spec,
        out_shape=jax.ShapeDtypeStruct((n_out, 1, kept), jnp.float32),
    )(valid, lhs, bias, rhs, sub)


def masked_lse(values, mask, axis):
    high = jnp.max(jnp.where(mask, values, floor_value), axis=axis)
    total = jnp.sum(
        jnp.where(mask, jnp.exp(values - jnp.expand_dims(high, axis)), 0.0), axis=axis
    )
    return jnp.where(jnp.any(mask, axis=axis), high + jnp.log(total), floor_value)


def log_add(first, second):
    high = jnp.maximum(first, second)
    return high + jnp.log(jnp.exp(first - high) + jnp.exp(second - high))


def body(src_points, dst_points, support, log_src_mass, log_dst_mass, dst_potential, n_row, n_col):
    row_count, dim_part, pts = src_points.shape
    col_count = dst_points.shape[0]
    col_id = lax.axis_index("col")

    dst_copies = jnp.broadcast_to(dst_points[None], (n_row,) + dst_points.shape)
    dst_recv = lax.all_to_all(dst_copies, "row", 0, 0, tiled=True)

    dev_of = support // col_count
    touches = jnp.any(
        dev_of[:, :, None] == jnp.arange(n_col, dtype=jnp.int32)[None, None, :], axis=1
    )
    rank = jnp.cumsum(touches.astype(jnp.int32), axis=0) - 1
    onehot = touches.T[:, None, :] & (
        rank.T[:, None, :] == jnp.arange(SLOTS, dtype=jnp.int32)[None, :, None]
    )
    table = jnp.sum(
        onehot.astype(jnp.int32) * jnp.arange(row_count, dtype=jnp.int32)[None, None, :], axis=2
    )
    slot_ok = jnp.any(onehot, axis=2)

    send = jnp.take(src_points, table.reshape(-1), axis=0).reshape(
        n_col, SLOTS, dim_part, pts
    ) * 4
    dst_recv, send = lax.optimization_barrier((dst_recv, send))
    recv = lax.all_to_all(send, "col", 0, 0, tiled=True)
    src_four = recv.transpose(1, 0, 2, 3).reshape(SLOTS, n_col * dim_part, pts)

    dst_full = dst_recv.transpose(1, 0, 2, 3).reshape(col_count, -1, pts)
    my_table = lax.dynamic_index_in_dim(table, col_id, 0, keepdims=False)
    my_ok = lax.dynamic_index_in_dim(slot_ok, col_id, 0, keepdims=False)
    my_support = jnp.take(support, my_table, axis=0)
    valid = my_ok[:, None] & jnp.any(
        my_support[:, None, :]
        == (col_id * col_count + jnp.arange(col_count, dtype=jnp.int32))[None, :, None],
        axis=2,
    )

    src_vals = src_four.astype(jnp.float32)
    src_sq = jnp.sum(src_vals * src_vals, axis=1) / 16.0
    dst_vals = dst_full.astype(jnp.float32)
    dst_sq = jnp.sum(dst_vals * dst_vals, axis=1)

    valid_int = valid.astype(jnp.int32)
    dst_bias = (2.0 * dst_potential - 2.0 * dst_sq)[:, :, None]
    row_local = tile_lse(
        valid_int.reshape(-1), dst_full, dst_bias, src_four, (2.0 * src_sq)[:, None, :]
    )[:, 0, :]
    row_local = jnp.where(my_ok[:, None], row_local, floor_value)

    row_all = lax.all_gather(row_local, "col", axis=0, tiled=False)
    owner = onehot.transpose(2, 0, 1)
    whole = masked_lse(
        jnp.broadcast_to(row_all[None], (row_count, n_col, SLOTS, pts)).reshape(row_count, n_col * SLOTS, pts),
        owner.reshape(row_count, n_col * SLOTS)[:, :, None],
        axis=1,
    )
    src_new = blur_scale * (log_src_mass - whole)

    my_pot = jnp.take(src_new, my_table, axis=0)
    src_bias = (2.0 * my_pot - 2.0 * src_sq)[:, None, :]
    col_local = tile_lse(
        valid_int.T.reshape(-1), src_four, src_bias, dst_full, (2.0 * dst_sq)[:, None, :], True
    )[:, 0, :]

    col_copies = jnp.broadcast_to(col_local[None], (n_row,) + col_local.shape)
    col_all = lax.all_to_all(col_copies, "row", 0, 0, tiled=True)
    col_high = jnp.max(col_all, axis=0)
    col_whole = col_high + jnp.log(jnp.sum(jnp.exp(col_all - col_high[None]), axis=0))
    dst_new = blur_scale * (log_dst_mass - col_whole)
    return (src_new, dst_new)


def solution(mesh):
    n_row = mesh.shape["row"]
    n_col = mesh.shape["col"]
    return jax.shard_map(
        functools.partial(body, n_row=n_row, n_col=n_col),
        mesh=mesh,
        in_specs=(
            P("row", "col", None),
            P("col", "row", None),
            P("row", None),
            P("row", None),
            P("col", None),
            P("col", None),
        ),
        out_specs=(P("row", None), P("col", None)),
        check_vma=False,
    )
```

```python
import functools

import jax
import jax.numpy as jnp
from jax import lax
from jax.experimental import pallas as pl
from jax.experimental.pallas import tpu as pltpu
from jax.sharding import PartitionSpec as P

blur_scale = 0.5
floor_value = -1e30
SLOTS = 3
CHUNK = 256


def tile_kernel(valid_ref, lhs_ref, bias_ref, rhs_ref, sub_ref, out_ref, acc_high, acc_total, dense_bias):
    outer = pl.program_id(0)
    inner = pl.program_id(1)
    n_inner = pl.num_programs(1)
    reduced = lhs_ref.shape[2]
    kept = rhs_ref.shape[2]

    @pl.when(inner == 0)
    def _():
        acc_high[...] = jnp.full((1, kept), floor_value, jnp.float32)
        acc_total[...] = jnp.zeros((1, kept), jnp.float32)

    @pl.when(valid_ref[outer * n_inner + inner] > 0)
    def _():
        rhs = rhs_ref[0]

        def chunk(ci, carry):
            high, total = carry
            start = pl.multiple_of(ci * CHUNK, CHUNK)
            left = lhs_ref[0, :, pl.ds(start, CHUNK)]
            vals = lax.dot_general(
                left, rhs, (((0,), (0,)), ((), ())), preferred_element_type=jnp.float32
            )
            if dense_bias:
                bias_row = jnp.broadcast_to(bias_ref[0, :, pl.ds(start, CHUNK)], (8, CHUNK))
                vals = vals + jnp.transpose(bias_row)[:, 0:1]
            else:
                vals = vals + bias_ref[0, pl.ds(start, CHUNK), :]
            new_high = jnp.maximum(high, jnp.max(vals, axis=0, keepdims=True))
            total = total * jnp.exp(high - new_high) + jnp.sum(
                jnp.exp(vals - new_high), axis=0, keepdims=True
            )
            return new_high, total

        start = (
            jnp.full((1, kept), floor_value, jnp.float32),
            jnp.zeros((1, kept), jnp.float32),
        )
        high, total = lax.fori_loop(0, reduced // CHUNK, chunk, start, unroll=True)
        old_high = acc_high[...]
        new_high = jnp.maximum(old_high, high)
        acc_total[...] = acc_total[...] * jnp.exp(old_high - new_high) + total * jnp.exp(
            high - new_high
        )
        acc_high[...] = new_high

    @pl.when(inner == n_inner - 1)
    def _():
        total = acc_total[...]
        found = total > 0.0
        whole = acc_high[...] + jnp.log(jnp.where(found, total, 1.0))
        out_ref[0] = jnp.where(found, whole - sub_ref[0], floor_value)


def tile_lse(valid, lhs, bias, rhs, sub, dense_bias=False):
    n_in, depth, reduced = lhs.shape
    n_out, _, kept = rhs.shape
    grid_spec = pltpu.PrefetchScalarGridSpec(
        num_scalar_prefetch=1,
        grid=(n_out, n_in),
        in_specs=[
            pl.BlockSpec((1, depth, reduced), lambda o, n, v: (n, 0, 0)),
            pl.BlockSpec((1,) + bias.shape[1:], lambda o, n, v: (n, 0, 0)),
            pl.BlockSpec((1, depth, kept), lambda o, n, v: (o, 0, 0)),
            pl.BlockSpec((1, 1, kept), lambda o, n, v: (o, 0, 0)),
        ],
        out_specs=pl.BlockSpec((1, 1, kept), lambda o, n, v: (o, 0, 0)),
        scratch_shapes=[pltpu.VMEM((1, kept), jnp.float32), pltpu.VMEM((1, kept), jnp.float32)],
    )
    return pl.pallas_call(
        functools.partial(tile_kernel, dense_bias=dense_bias),
        grid_spec=grid_spec,
        out_shape=jax.ShapeDtypeStruct((n_out, 1, kept), jnp.float32),
    )(valid, lhs, bias, rhs, sub)


def masked_lse(values, mask, axis):
    high = jnp.max(jnp.where(mask, values, floor_value), axis=axis)
    total = jnp.sum(
        jnp.where(mask, jnp.exp(values - jnp.expand_dims(high, axis)), 0.0), axis=axis
    )
    return jnp.where(jnp.any(mask, axis=axis), high + jnp.log(total), floor_value)


def log_add(first, second):
    high = jnp.maximum(first, second)
    return high + jnp.log(jnp.exp(first - high) + jnp.exp(second - high))


def body(src_points, dst_points, support, log_src_mass, log_dst_mass, dst_potential, n_row, n_col):
    row_count, dim_part, pts = src_points.shape
    col_count = dst_points.shape[0]
    col_id = lax.axis_index("col")

    dst_copies = jnp.broadcast_to(dst_points[None], (n_row,) + dst_points.shape)
    dst_recv = lax.all_to_all(dst_copies, "row", 0, 0, tiled=True)

    dev_of = support // col_count
    touches = jnp.any(
        dev_of[:, :, None] == jnp.arange(n_col, dtype=jnp.int32)[None, None, :], axis=1
    )
    rank = jnp.cumsum(touches.astype(jnp.int32), axis=0) - 1
    onehot = touches.T[:, None, :] & (
        rank.T[:, None, :] == jnp.arange(SLOTS, dtype=jnp.int32)[None, :, None]
    )
    table = jnp.sum(
        onehot.astype(jnp.int32) * jnp.arange(row_count, dtype=jnp.int32)[None, None, :], axis=2
    )
    slot_ok = jnp.any(onehot, axis=2)

    send = jnp.take(src_points, table.reshape(-1), axis=0).reshape(
        n_col, SLOTS, dim_part, pts
    ) * 4
    dst_recv, send = lax.optimization_barrier((dst_recv, send))
    recv = lax.all_to_all(send, "col", 0, 0, tiled=True)
    src_four = recv.transpose(1, 0, 2, 3).reshape(SLOTS, n_col * dim_part, pts)

    dst_full = dst_recv.transpose(1, 0, 2, 3).reshape(col_count, -1, pts)
    my_table = lax.dynamic_index_in_dim(table, col_id, 0, keepdims=False)
    my_ok = lax.dynamic_index_in_dim(slot_ok, col_id, 0, keepdims=False)
    my_support = jnp.take(support, my_table, axis=0)
    valid = my_ok[:, None] & jnp.any(
        my_support[:, None, :]
        == (col_id * col_count + jnp.arange(col_count, dtype=jnp.int32))[None, :, None],
        axis=2,
    )

    src_vals = src_four.astype(jnp.float32)
    src_sq = jnp.sum(src_vals * src_vals, axis=1) / 16.0
    dst_vals = dst_full.astype(jnp.float32)
    dst_sq = jnp.sum(dst_vals * dst_vals, axis=1)

    valid_int = valid.astype(jnp.int32)
    dst_bias = (2.0 * dst_potential - 2.0 * dst_sq)[:, :, None]
    row_local = tile_lse(
        valid_int.reshape(-1), dst_full, dst_bias, src_four, (2.0 * src_sq)[:, None, :]
    )[:, 0, :]

    row_all = lax.all_gather(row_local, "col", axis=0, tiled=False)
    owner = onehot.transpose(2, 0, 1)
    whole = masked_lse(
        jnp.broadcast_to(row_all[None], (row_count, n_col, SLOTS, pts)).reshape(row_count, n_col * SLOTS, pts),
        owner.reshape(row_count, n_col * SLOTS)[:, :, None],
        axis=1,
    )
    src_new = blur_scale * (log_src_mass - whole)

    my_pot = jnp.take(src_new, my_table, axis=0)
    src_bias = (2.0 * my_pot - 2.0 * src_sq)[:, None, :]
    col_local = tile_lse(
        valid_int.T.reshape(-1), src_four, src_bias, dst_full, (2.0 * dst_sq)[:, None, :], True
    )[:, 0, :]

    col_copies = jnp.broadcast_to(col_local[None], (n_row,) + col_local.shape)
    col_all = lax.all_to_all(col_copies, "row", 0, 0, tiled=True)
    col_high = jnp.max(col_all, axis=0)
    col_whole = col_high + jnp.log(jnp.sum(jnp.exp(col_all - col_high[None]), axis=0))
    dst_new = blur_scale * (log_dst_mass - col_whole)
    return (src_new, dst_new)


def solution(mesh):
    n_row = mesh.shape["row"]
    n_col = mesh.shape["col"]
    return jax.shard_map(
        functools.partial(body, n_row=n_row, n_col=n_col),
        mesh=mesh,
        in_specs=(
            P("row", "col", None),
            P("col", "row", None),
            P("row", None),
            P("row", None),
            P("col", None),
            P("col", None),
        ),
        out_specs=(P("row", None), P("col", None)),
        check_vma=False,
    )
```
